1024 devices in a mesh: grp: 32 (over y, x_lo), slab: 32 (over z, x_hi, core).
Axes of the slice: x: 8 (x_hi: 2, x_lo: 4; x = x_hi * 4 + x_lo), y: 8, z: 8, core: 2. Of those that a mesh axis runs over, the one named last changes fastest.
Arguments:
- tiles: bfloat16 [32768, 2, 8, 512], P(('grp', 'slab')), may hold values from -6 to 6
- conv_weight: bfloat16 [576, 64], replicated, may hold values from -0.25 to 0.25
- assignment: int32 [32768, 1], P(('grp', 'slab')), may hold values from 0 to 31; in each aligned block of 32 rows (0 to 31, 32 to 63, ...) at most 2 rows name the same one
- occupancy: int32 [32768], P(('grp', 'slab')), may hold values 0 or 1
- cotangent: bfloat16 [65536, 2, 8, 512], P(('grp', 'slab')), may hold values from -6 to 6
Outputs:
- activations: bfloat16 [65536, 2, 8, 512], P(('grp', 'slab'))
- input_grad: bfloat16 [32768, 2, 8, 512], P(('grp', 'slab'))
- weight_grad: float32 [576, 64], replicated
The draws below stay inside these ranges and needn't reach their ends.
Inputs may be any that keep to these rules, and one draw needn't show every extreme that they name: `assignment`: the trainer of a tile, an index along slab within the owner's group; among the 32 tiles of one owner at most 2 have the same trainer. `occupancy`: only tiles with 1 are trained.
All inputs are finite; a program needn't handle non-finite values. No bound on the sum of `occupancy` on one device may be relied on, other than what follows from the above.
Results may differ from the reference program's by a relative error of at most 0.0049.
Values may be sent and summed in bfloat16 or wider, within the bound.
No kernel may reach another device: no remote copies, remote signals or barrier semaphores. Data moves between devices by JAX's collectives and lax.ppermute only.
A program may use at most 32 MiB of HBM per device.

```python
import math
import jax
import jax.numpy as jnp
import numpy as np
from jax import lax

C = 64
TD = 2
TH = 8
TW = 8
TPD = 32
CAP = 2
SLOTS = 64
TILES_ALL = 32768
SLOTS_ALL = 65536
N_GRP = 32
N_SLAB = 32


def touch_ends(values, rng, least, top_value):
    longest = values.shape.index(max(values.shape))
    spots = []
    for shift in (0, 1):
        where = [jax.random.randint(jax.random.fold_in(rng, axis), (), 0, length) for axis, length in enumerate(values.shape)]
        where[longest] = (where[longest] + shift) % values.shape[longest]
        spots.append(tuple(where))
    return values.at[spots[0]].set(least).at[spots[1]].set(top_value)


def level_of(stream_key, shape, cuts, smallest, largest):
    gain, own = 1.0, jax.random.fold_in(stream_key, 6)
    for dim, parts in cuts:
        heights = jnp.exp(jax.random.uniform(jax.random.fold_in(own, dim), (parts,), jnp.float32, smallest / len(cuts), largest / len(cuts)))
        gain = gain * jnp.repeat(heights, shape[dim] // parts).reshape([-1 if axis == dim else 1 for axis in range(len(shape))])
    return gain


def routed_block(key, own, number, rows, number_of, top, most, lean):
    ranking = jax.random.permutation(key, number_of)
    packed, ordinary = shares(number_of, rows * top, most, lean, True), shares(number_of, rows * top, most, lean, False)
    places = jnp.arange(number_of)

    def named(lengths, offset_by):
        used = int((lengths > 0).sum())
        fixed = max(1, used // 4)
        moved = fixed + (places - fixed + offset_by * (used - fixed)) % max(1, number_of - fixed)
        return jnp.zeros((number_of,), jnp.int32).at[ranking[jnp.where(places < fixed, places, moved)]].set(jnp.asarray(lengths, jnp.int32))

    lengths = jnp.where(number % 4 == 0, named(packed, number // 4), named(ordinary, number - number // 4 - 1))
    mixed = jax.random.permutation(jax.random.fold_in(own, 3), number_of)
    giver, receiver = mixed[0:number_of // 2 * 2:2], mixed[1:number_of // 2 * 2:2]
    room = jnp.minimum(lengths[giver] - 1, most - lengths[receiver]) // 2
    room = jnp.where((giver == ranking[0]) | (receiver == ranking[0]) | (lengths[receiver] == 0), 0, jnp.maximum(room, 0))
    moved = jax.random.randint(jax.random.fold_in(own, 4), (number_of // 2,), 0, 1 << 20) % (room + 1)
    lengths = lengths.at[giver].add(-moved).at[receiver].add(moved)
    labels = jnp.searchsorted(jnp.cumsum(lengths), jnp.arange(rows * top), side="right").astype(jnp.int32)
    grid = labels.reshape(top, rows).T
    grid = grid[jax.random.permutation(jax.random.fold_in(own, 1), rows)]
    offset_by = jax.random.randint(jax.random.fold_in(own, 2), (rows, 1), 0, top)
    return jnp.take_along_axis(grid, (jnp.arange(top)[None, :] + offset_by) % top, axis=1)


def shares(number_of, total, most, skew, full):
    weights = [(1 << 20) // math.isqrt(standing ** skew) + 1 for standing in range(1, number_of + 1)]
    largest = most if full else min(most, max(-(-total // number_of), total * weights[0] // sum(weights)))
    least = 1 if total - largest >= number_of - 1 else 0
    given, rest = [largest] + [least] * (number_of - 1), total - largest - least * (number_of - 1)
    while rest > 0:
        candidates = [i for i in range(1, number_of) if given[i] < largest] or [i for i in range(1, number_of) if given[i] < most]
        whole, budget = sum([weights[i] for i in candidates]), rest
        for i in candidates:
            extra = min(most - given[i], max(1, budget * weights[i] // whole), rest)
            given[i] = given[i] + extra
            rest = rest - extra
    return np.array(given)


def scatter_about(rng, extent, scale, reach, split=(), kind=jnp.bfloat16):
    drawn = jax.random.normal(rng, extent, jnp.float32) * scale
    if len(split) > 0:
        drawn = level_of(rng, extent, split, -0.22, 0.18) * drawn
    return jnp.clip(drawn, min=-reach, max=reach).astype(kind)


def setup_inputs(seed: int = 0) -> dict:
    key_list = jax.random.split(jax.random.key(seed), 6)
    tiles = scatter_about(key_list[0], (TILES_ALL, TD, TH, TW * C), 1.0, 6.0, ((0, 1024),))
    conv_weight = scatter_about(key_list[1], (9 * C, C), (9 * C) ** -0.5, 0.25)
    assignment_keys = jax.random.split(jax.random.fold_in(key_list[2], 1), TILES_ALL // TPD)
    assignment_turns = jax.random.permutation(jax.random.fold_in(key_list[2], 3), TILES_ALL // TPD)
    assignment = jax.vmap(lambda own, number: routed_block(jax.random.fold_in(key_list[2], 2), own, number, TPD, N_SLAB, 1, CAP, 2))(assignment_keys, assignment_turns).reshape((TILES_ALL, 1))
    occupancy = touch_ends((jax.random.randint(key_list[3], (TILES_ALL,), 0, 4) < 3).astype(jnp.int32), jax.random.fold_in(key_list[3], 1), 0, 1)
    cotangent = scatter_about(key_list[4], (SLOTS_ALL, TD, TH, TW * C), 1.0, 6.0, ((0, 1024),))
    return dict(tiles=tiles, conv_weight=conv_weight, assignment=assignment, occupancy=occupancy, cotangent=cotangent)


def tile_ranks(targets):
    count = targets.shape[0]
    same = targets[:, None] == targets[None, :]
    before = jnp.arange(count)[None, :] < jnp.arange(count)[:, None]
    return lax.optimization_barrier(jnp.sum((same & before).astype(jnp.int32), axis=1)).astype(jnp.int32)

def layer_math(tile_set, kernel, upstream, mask):
    count = tile_set.shape[0]
    inputs = tile_set.astype(jnp.float32).reshape(count, TD, TH, TW, C)
    padded = jnp.pad(inputs, ((0, 0), (0, 0), (1, 1), (1, 1), (0, 0)))
    taps = kernel.astype(jnp.float32).reshape(9, C, C)
    pre = jnp.zeros((count, TD, TH, TW, C), jnp.float32)
    for row in range(3):
        for col in range(3):
            window = padded[:, :, row:row + TH, col:col + TW, :]
            pre = pre + jnp.einsum('ndhwc,co->ndhwo', window, taps[3 * row + col])
    sig = jax.nn.sigmoid(pre)
    act = (pre * sig).astype(jnp.bfloat16)
    slope = sig * (1.0 + pre * (1.0 - sig))
    upstream5 = upstream.astype(jnp.float32).reshape(count, TD, TH, TW, C)
    maskf = mask.astype(jnp.float32)[:, None, None, None, None]
    grad_pre = (upstream5 * slope * maskf).astype(jnp.bfloat16).astype(jnp.float32)
    padded_grad = jnp.pad(grad_pre, ((0, 0), (0, 0), (1, 1), (1, 1), (0, 0)))
    back = jnp.zeros((count, TD, TH, TW, C), jnp.float32)
    pieces = []
    for row in range(3):
        for col in range(3):
            window = padded[:, :, row:row + TH, col:col + TW, :]
            pieces.append(jnp.einsum('ndhwc,ndhwo->co', window, grad_pre))
            shifted = padded_grad[:, :, 2 - row:2 - row + TH, 2 - col:2 - col + TW, :]
            back = back + jnp.einsum('ndhwo,co->ndhwc', shifted, taps[3 * row + col])
    back = (back * maskf).astype(jnp.bfloat16)
    wgrad = jnp.stack(pieces).reshape(9 * C, C)
    return (act.reshape(count, TD, TH, TW * C), back.reshape(count, TD, TH, TW * C), wgrad)

def reference(tiles, conv_weight, assignment, occupancy, cotangent):
    tiles_g = tiles.reshape(N_GRP, N_SLAB * TPD, TD, TH, TW * C)
    assign_g = assignment.reshape(N_GRP, N_SLAB, TPD)
    occ_g = occupancy.reshape(N_GRP, N_SLAB * TPD)
    cot_g = cotangent.reshape(N_GRP, N_SLAB * SLOTS, TD, TH, TW * C)

    def group_part(items):
        tile_set, targets, mask, upstream_slots = items
        ranks = jax.vmap(tile_ranks)(targets)
        owners = jnp.arange(N_SLAB, dtype=jnp.int32)[:, None]
        index = (targets * (N_SLAB * CAP) + owners * CAP + ranks).reshape(-1).astype(jnp.int32)
        upstream = jnp.take(upstream_slots, index, axis=0)
        act, back, wgrad = layer_math(tile_set, conv_weight, upstream, mask)
        kept = act * mask.astype(jnp.bfloat16)[:, None, None, None]
        slots_out = jnp.zeros_like(upstream_slots).at[index].set(kept)
        return (slots_out, back, wgrad)
    acts, backs, wgrads = lax.map(group_part, (tiles_g, assign_g, occ_g, cot_g))
    scale = 1.0 / math.sqrt(TILES_ALL * TD * TH * TW)
    weight_grad = lax.optimization_barrier(jnp.sum(wgrads, axis=0)) * scale
    return (acts.reshape(SLOTS_ALL, TD, TH, TW * C), backs.reshape(TILES_ALL, TD, TH, TW * C), weight_grad)
```

```python
import math

import jax
import jax.numpy as jnp
from jax import lax
from jax.sharding import PartitionSpec as P

C = 64
TD = 2
TH = 8
TW = 8


def cut_along(x, dim, size):
    before, after = (x.shape[:dim], x.shape[dim + 1 :])
    return jnp.moveaxis(x.reshape(*before, size, -1, *after), dim, 0)


def sent_and_summed(x, axis, dim):
    size = lax.axis_size(axis)
    pieces = lax.all_to_all(cut_along(x, dim, size), axis, 0, 0, tiled=True)
    return jnp.sum(pieces, axis=0)


def sent_to_all(x, axis):
    size = lax.axis_size(axis)
    return lax.all_to_all(jnp.broadcast_to(x[None], (size, *x.shape)), axis, 0, 0, tiled=True)


def over_copies(x, axis):
    everything = sent_to_all(x, axis)
    return jnp.sum(everything, axis=0)


def joined_along(pieces, dim):
    pieces = jnp.moveaxis(pieces, 0, dim)
    dims = pieces.shape
    return pieces.reshape(*dims[:dim], dims[dim] * dims[dim + 1], *dims[dim + 2 :])


def gathered_copies(x, axis, dim):
    return joined_along(sent_to_all(x, axis), dim)


def conv_forward(planes, kernel):
    return lax.conv_general_dilated(
        planes,
        kernel,
        (1, 1),
        ((1, 1), (1, 1)),
        dimension_numbers=("NHWC", "HWIO", "NHWC"),
        preferred_element_type=jnp.float32,
    )


def conv_input_grad(grad_planes, kernel):
    flipped = jnp.transpose(kernel[::-1, ::-1, :, :], (0, 1, 3, 2))
    return lax.conv_general_dilated(
        grad_planes,
        flipped,
        (1, 1),
        ((1, 1), (1, 1)),
        dimension_numbers=("NHWC", "HWIO", "NHWC"),
        preferred_element_type=jnp.float32,
    )


def conv_kernel_grad(planes, grad_planes):
    return lax.conv_general_dilated(
        planes,
        grad_planes,
        (1, 1),
        ((1, 1), (1, 1)),
        dimension_numbers=("CHWN", "IHWO", "HWNC"),
        preferred_element_type=jnp.float32,
    )


def layer_local(tile_set, kernel, upstream, mask):
    count = tile_set.shape[0]
    planes = tile_set.reshape(count * TD, TH, TW, C)
    pre = conv_forward(planes, kernel)
    sig = jax.nn.sigmoid(pre)
    act = (pre * sig).astype(jnp.bfloat16).reshape(count, TD, TH, TW * C)
    slope = sig * (1.0 + pre * (1.0 - sig))
    grad_pre = upstream.reshape(count * TD, TH, TW, C).astype(jnp.float32) * slope
    plane_mask = jnp.repeat(mask, TD)
    grad_pre = grad_pre * plane_mask[:, None, None, None]
    grad_pre = grad_pre.astype(jnp.bfloat16)
    back = conv_input_grad(grad_pre, kernel)
    wgrad = conv_kernel_grad(planes, grad_pre).reshape(9 * C, C)
    back = back * plane_mask[:, None, None, None]
    return (act, back.astype(jnp.bfloat16).reshape(count, TD, TH, TW * C), wgrad)


def local(tiles, conv_weight, assignment, occupancy, cotangent):
    n_slab = lax.axis_size("slab")
    n_group = lax.axis_size("grp")
    per_owner = tiles.shape[0]
    capacity = max(2, -(-per_owner // n_slab))
    slot_count = n_slab * capacity
    targets = assignment[:, 0]
    same = targets[:, None] == targets[None, :]
    before = jnp.arange(per_owner)[None, :] < jnp.arange(per_owner)[:, None]
    ranks = jnp.sum((same & before).astype(jnp.int32), axis=1)
    slot_ids = targets * capacity + ranks
    placer = (
        (jnp.arange(slot_count)[:, None] == slot_ids[None, :]) & (occupancy[None, :] == 1)
    ).astype(jnp.bfloat16)
    kernel = conv_weight.reshape(3, 3, C, C)
    upstream_slots = lax.all_to_all(cotangent, "slab", split_axis=0, concat_axis=0, tiled=True)
    upstream = jnp.einsum(
        "sk,sdhx->kdhx", placer, upstream_slots, preferred_element_type=jnp.float32
    ).astype(jnp.bfloat16)
    mask = occupancy.astype(jnp.float32)
    act_tiles, input_grad, wgrad = layer_local(tiles, kernel, upstream, mask)
    outgoing = jnp.einsum(
        "sk,kdhx->sdhx", placer, act_tiles, preferred_element_type=jnp.float32
    ).astype(jnp.bfloat16)
    activations = lax.all_to_all(outgoing, "slab", split_axis=0, concat_axis=0, tiled=True)
    summed = lax.psum(wgrad, ("grp", "slab"))
    scale = 1.0 / math.sqrt(per_owner * n_group * n_slab * TD * TH * TW)
    return (activations, input_grad, summed * scale)


def solution(mesh):
    in_specs = (
        P(("grp", "slab"), None, None, None),
        P(),
        P(("grp", "slab"), None),
        P(("grp", "slab")),
        P(("grp", "slab"), None, None, None),
    )
    out_specs = (P(("grp", "slab"), None, None, None), P(("grp", "slab"), None, None, None), P())
    return jax.shard_map(local, mesh=mesh, in_specs=in_specs, out_specs=out_specs, check_vma=False)
```

```python
import math

import jax
import jax.numpy as jnp
from jax import lax
from jax.sharding import PartitionSpec as P

C = 64
TD = 2
TH = 8
TW = 8


def cut_along(x, dim, size):
    before, after = (x.shape[:dim], x.shape[dim + 1 :])
    return jnp.moveaxis(x.reshape(*before, size, -1, *after), dim, 0)


def sent_and_summed(x, axis, dim):
    size = lax.axis_size(axis)
    pieces = lax.all_to_all(cut_along(x, dim, size), axis, 0, 0, tiled=True)
    return jnp.sum(pieces, axis=0)


def sent_to_all(x, axis):
    size = lax.axis_size(axis)
    return lax.all_to_all(jnp.broadcast_to(x[None], (size, *x.shape)), axis, 0, 0, tiled=True)


def over_copies(x, axis):
    everything = sent_to_all(x, axis)
    return jnp.sum(everything, axis=0)


def joined_along(pieces, dim):
    pieces = jnp.moveaxis(pieces, 0, dim)
    dims = pieces.shape
    return pieces.reshape(*dims[:dim], dims[dim] * dims[dim + 1], *dims[dim + 2 :])


def gathered_copies(x, axis, dim):
    return joined_along(sent_to_all(x, axis), dim)


def conv_forward(planes, kernel):
    return lax.conv_general_dilated(
        planes,
        kernel,
        (1, 1),
        ((1, 1), (1, 1)),
        dimension_numbers=("NHWC", "HWIO", "NHWC"),
        preferred_element_type=jnp.float32,
    )


def conv_input_grad(grad_planes, kernel):
    flipped = jnp.transpose(kernel[::-1, ::-1, :, :], (0, 1, 3, 2))
    return lax.conv_general_dilated(
        grad_planes,
        flipped,
        (1, 1),
        ((1, 1), (1, 1)),
        dimension_numbers=("NHWC", "HWIO", "NHWC"),
        preferred_element_type=jnp.float32,
    )


def conv_kernel_grad(planes, grad_planes):
    return lax.conv_general_dilated(
        planes,
        grad_planes,
        (1, 1),
        ((1, 1), (1, 1)),
        dimension_numbers=("CHWN", "IHWO", "HWNC"),
        preferred_element_type=jnp.float32,
    )


def layer_local(tile_set, kernel, upstream, mask):
    count = tile_set.shape[0]
    planes = tile_set.reshape(count * TD, TH, TW, C)
    pre = conv_forward(planes, kernel)
    sig = jax.nn.sigmoid(pre)
    act = (pre * sig).astype(jnp.bfloat16).reshape(count, TD, TH, TW * C)
    slope = sig * (1.0 + pre * (1.0 - sig))
    grad_pre = upstream.reshape(count * TD, TH, TW, C).astype(jnp.float32) * slope
    plane_mask = jnp.repeat(mask, TD)
    grad_pre = grad_pre * plane_mask[:, None, None, None]
    grad_pre = grad_pre.astype(jnp.bfloat16)
    back = conv_input_grad(grad_pre, kernel)
    wgrad = conv_kernel_grad(planes, grad_pre).reshape(9 * C, C)
    back = back * plane_mask[:, None, None, None]
    return (act, back.astype(jnp.bfloat16).reshape(count, TD, TH, TW * C), wgrad)


def local(tiles, conv_weight, assignment, occupancy, cotangent):
    n_slab = lax.axis_size("slab")
    n_group = lax.axis_size("grp")
    per_owner = tiles.shape[0]
    capacity = max(2, -(-per_owner // n_slab))
    slot_count = n_slab * capacity
    targets = assignment[:, 0]
    same = targets[:, None] == targets[None, :]
    before = jnp.arange(per_owner)[None, :] < jnp.arange(per_owner)[:, None]
    ranks = jnp.sum((same & before).astype(jnp.int32), axis=1)
    slot_ids = targets * capacity + ranks
    placer = (
        (jnp.arange(slot_count)[:, None] == slot_ids[None, :]) & (occupancy[None, :] == 1)
    ).astype(jnp.bfloat16)
    kernel = conv_weight.reshape(3, 3, C, C)
    upstream_slots = lax.all_to_all(cotangent, "slab", split_axis=0, concat_axis=0, tiled=True)
    upstream = jnp.einsum(
        "sk,sdhx->kdhx", placer, upstream_slots, preferred_element_type=jnp.float32
    ).astype(jnp.bfloat16)
    mask = occupancy.astype(jnp.float32)
    act_tiles, input_grad, wgrad = layer_local(tiles, kernel, upstream, mask)
    outgoing = jnp.einsum(
        "sk,kdhx->sdhx", placer, act_tiles, preferred_element_type=jnp.float32
    ).astype(jnp.bfloat16)
    flat_w = wgrad.reshape(n_slab, -1)
    high = flat_w.astype(jnp.bfloat16)
    low = (flat_w - high.astype(jnp.float32)).astype(jnp.bfloat16)
    act_rows = outgoing.reshape(n_slab, -1)
    act_width = act_rows.shape[1]
    share_width = flat_w.shape[1]
    payload = jnp.concatenate([act_rows, high, low], axis=1)
    arrived = lax.all_to_all(payload, "slab", split_axis=0, concat_axis=0, tiled=True)
    activations = arrived[:, :act_width].reshape(outgoing.shape)
    got_high = arrived[:, act_width : act_width + share_width].astype(jnp.float32)
    got_low = arrived[:, act_width + share_width :].astype(jnp.float32)
    share = jnp.sum(got_high, axis=0) + jnp.sum(got_low, axis=0)
    share = over_copies(share, "grp")
    summed = gathered_copies(share, "slab", 0).reshape(9 * C, C)
    scale = 1.0 / math.sqrt(per_owner * n_group * n_slab * TD * TH * TW)
    return (activations, input_grad, summed * scale)


def solution(mesh):
    in_specs = (
        P(("grp", "slab"), None, None, None),
        P(),
        P(("grp", "slab"), None),
        P(("grp", "slab")),
        P(("grp", "slab"), None, None, None),
    )
    out_specs = (P(("grp", "slab"), None, None, None), P(("grp", "slab"), None, None, None), P())
    return jax.shard_map(local, mesh=mesh, in_specs=in_specs, out_specs=out_specs, check_vma=False)
```

```python
import math

import jax
import jax.numpy as jnp
from jax import lax
from jax.sharding import PartitionSpec as P

C = 64
TD = 2
TH = 8
TW = 8


def cut_along(x, dim, size):
    before, after = (x.shape[:dim], x.shape[dim + 1 :])
    return jnp.moveaxis(x.reshape(*before, size, -1, *after), dim, 0)


def sent_and_summed(x, axis, dim):
    size = lax.axis_size(axis)
    pieces = lax.all_to_all(cut_along(x, dim, size), axis, 0, 0, tiled=True)
    return jnp.sum(pieces, axis=0)


def sent_to_all(x, axis):
    size = lax.axis_size(axis)
    return lax.all_to_all(jnp.broadcast_to(x[None], (size, *x.shape)), axis, 0, 0, tiled=True)


def over_copies(x, axis):
    everything = sent_to_all(x, axis)
    return jnp.sum(everything, axis=0)


def joined_along(pieces, dim):
    pieces = jnp.moveaxis(pieces, 0, dim)
    dims = pieces.shape
    return pieces.reshape(*dims[:dim], dims[dim] * dims[dim + 1], *dims[dim + 2 :])


def gathered_copies(x, axis, dim):
    return joined_along(sent_to_all(x, axis), dim)


def conv_forward(planes, kernel):
    return lax.conv_general_dilated(
        planes,
        kernel,
        (1, 1),
        ((1, 1), (1, 1)),
        dimension_numbers=("NHWC", "HWIO", "NHWC"),
        preferred_element_type=jnp.float32,
    )


def conv_input_grad(grad_planes, kernel):
    flipped = jnp.transpose(kernel[::-1, ::-1, :, :], (0, 1, 3, 2))
    return lax.conv_general_dilated(
        grad_planes,
        flipped,
        (1, 1),
        ((1, 1), (1, 1)),
        dimension_numbers=("NHWC", "HWIO", "NHWC"),
        preferred_element_type=jnp.float32,
    )


def conv_kernel_grad(planes, grad_planes):
    return lax.conv_general_dilated(
        planes,
        grad_planes,
        (1, 1),
        ((1, 1), (1, 1)),
        dimension_numbers=("CHWN", "IHWO", "HWNC"),
        preferred_element_type=jnp.float32,
    )


def local(tiles, conv_weight, assignment, occupancy, cotangent):
    n_slab = lax.axis_size("slab")
    n_group = lax.axis_size("grp")
    per_owner = tiles.shape[0]
    capacity = max(2, -(-per_owner // n_slab))
    slot_count = n_slab * capacity
    targets = assignment[:, 0]
    same = targets[:, None] == targets[None, :]
    before = jnp.arange(per_owner)[None, :] < jnp.arange(per_owner)[:, None]
    ranks = jnp.sum((same & before).astype(jnp.int32), axis=1)
    slot_ids = targets * capacity + ranks
    placer = (
        (jnp.arange(slot_count)[:, None] == slot_ids[None, :]) & (occupancy[None, :] == 1)
    ).astype(jnp.bfloat16)
    kernel = conv_weight.reshape(3, 3, C, C)
    upstream_slots = lax.all_to_all(cotangent, "slab", split_axis=0, concat_axis=0, tiled=True)

    count = per_owner
    planes = tiles.reshape(count * TD, TH, TW, C)
    pre = conv_forward(planes, kernel)
    sig = jax.nn.sigmoid(pre)
    act_tiles = (pre * sig).astype(jnp.bfloat16).reshape(count, TD, TH, TW * C)
    slope = sig * (1.0 + pre * (1.0 - sig))
    outgoing = jnp.einsum(
        "sk,kdhx->sdhx", placer, act_tiles, preferred_element_type=jnp.float32
    ).astype(jnp.bfloat16)
    outgoing, slope = lax.optimization_barrier((outgoing, slope))

    upstream = jnp.einsum(
        "sk,sdhx->kdhx", placer, upstream_slots, preferred_element_type=jnp.float32
    ).astype(jnp.bfloat16)
    mask = occupancy.astype(jnp.float32)
    plane_mask = jnp.repeat(mask, TD)
    grad_pre = upstream.reshape(count * TD, TH, TW, C).astype(jnp.float32) * slope
    grad_pre = grad_pre * plane_mask[:, None, None, None]
    grad_pre = grad_pre.astype(jnp.bfloat16)
    back = conv_input_grad(grad_pre, kernel)
    wgrad = conv_kernel_grad(planes, grad_pre).reshape(9 * C, C)
    back = back * plane_mask[:, None, None, None]
    input_grad = back.astype(jnp.bfloat16).reshape(count, TD, TH, TW * C)

    flat_w = wgrad.reshape(n_slab, -1)
    high = lax.reduce_precision(flat_w, exponent_bits=8, mantissa_bits=7)
    low = flat_w - high
    share_width = flat_w.shape[1]
    plane = TH * TW * C
    extra = -(-2 * share_width // plane)
    pair = jnp.concatenate([high, low], axis=1).astype(jnp.bfloat16)
    pair = jnp.pad(pair, ((0, 0), (0, extra * plane - 2 * share_width)))
    pair = pair.reshape(n_slab, extra, TH, TW * C)
    act_rows = outgoing.reshape(n_slab, capacity * TD, TH, TW * C)
    payload = jnp.concatenate([act_rows, pair], axis=1)
    arrived = lax.all_to_all(payload, "slab", split_axis=0, concat_axis=0, tiled=True)
    activations = arrived[:, : capacity * TD].reshape(outgoing.shape)
    got = arrived[:, capacity * TD :].reshape(n_slab, -1)[:, : 2 * share_width].astype(jnp.float32)
    share = jnp.sum(got[:, :share_width], axis=0) + jnp.sum(got[:, share_width:], axis=0)
    share = over_copies(share, "grp")
    summed = gathered_copies(share, "slab", 0).reshape(9 * C, C)
    scale = 1.0 / math.sqrt(per_owner * n_group * n_slab * TD * TH * TW)
    return (activations, input_grad, summed * scale)


def solution(mesh):
    in_specs = (
        P(("grp", "slab"), None, None, None),
        P(),
        P(("grp", "slab"), None),
        P(("grp", "slab")),
        P(("grp", "slab"), None, None, None),
    )
    out_specs = (P(("grp", "slab"), None, None, None), P(("grp", "slab"), None, None, None), P())
    return jax.shard_map(local, mesh=mesh, in_specs=in_specs, out_specs=out_specs, check_vma=False)
```

```python
import math

import jax
import jax.numpy as jnp
from jax import lax
from jax.sharding import PartitionSpec as P

C = 64
TD = 2
TH = 8
TW = 8


def cut_along(x, dim, size):
    before, after = (x.shape[:dim], x.shape[dim + 1 :])
    return jnp.moveaxis(x.reshape(*before, size, -1, *after), dim, 0)


def sent_and_summed(x, axis, dim):
    size = lax.axis_size(axis)
    pieces = lax.all_to_all(cut_along(x, dim, size), axis, 0, 0, tiled=True)
    return jnp.sum(pieces, axis=0)


def sent_to_all(x, axis):
    size = lax.axis_size(axis)
    return lax.all_to_all(jnp.broadcast_to(x[None], (size, *x.shape)), axis, 0, 0, tiled=True)


def over_copies(x, axis):
    everything = sent_to_all(x, axis)
    return jnp.sum(everything, axis=0)


def joined_along(pieces, dim):
    pieces = jnp.moveaxis(pieces, 0, dim)
    dims = pieces.shape
    return pieces.reshape(*dims[:dim], dims[dim] * dims[dim + 1], *dims[dim + 2 :])


def gathered_copies(x, axis, dim):
    return joined_along(sent_to_all(x, axis), dim)


def conv_forward(planes, kernel):
    return lax.conv_general_dilated(
        planes,
        kernel,
        (1, 1),
        ((1, 1), (1, 1)),
        dimension_numbers=("NHWC", "HWIO", "NHWC"),
        preferred_element_type=jnp.float32,
    )


def conv_input_grad(grad_planes, kernel):
    flipped = jnp.transpose(kernel[::-1, ::-1, :, :], (0, 1, 3, 2))
    return lax.conv_general_dilated(
        grad_planes,
        flipped,
        (1, 1),
        ((1, 1), (1, 1)),
        dimension_numbers=("NHWC", "HWIO", "NHWC"),
        preferred_element_type=jnp.float32,
    )


def conv_kernel_grad(planes, grad_planes):
    return lax.conv_general_dilated(
        planes,
        grad_planes,
        (1, 1),
        ((1, 1), (1, 1)),
        dimension_numbers=("CHWN", "IHWO", "HWNC"),
        preferred_element_type=jnp.float32,
    )


def local(tiles, conv_weight, assignment, occupancy, cotangent):
    n_slab = lax.axis_size("slab")
    n_group = lax.axis_size("grp")
    per_owner = tiles.shape[0]
    capacity = max(2, -(-per_owner // n_slab))
    slot_count = n_slab * capacity
    targets = assignment[:, 0]
    same = targets[:, None] == targets[None, :]
    before = jnp.arange(per_owner)[None, :] < jnp.arange(per_owner)[:, None]
    ranks = jnp.sum((same & before).astype(jnp.int32), axis=1)
    slot_ids = targets * capacity + ranks
    placer = (
        (jnp.arange(slot_count)[:, None] == slot_ids[None, :]) & (occupancy[None, :] == 1)
    ).astype(jnp.bfloat16)
    kernel = conv_weight.reshape(3, 3, C, C)
    upstream_slots = lax.all_to_all(cotangent, "slab", split_axis=0, concat_axis=0, tiled=True)

    count = per_owner
    planes = tiles.reshape(count * TD, TH, TW, C)
    pre = conv_forward(planes, kernel)
    sig = jax.nn.sigmoid(pre)
    act_tiles = (pre * sig).astype(jnp.bfloat16).reshape(count, TD, TH, TW * C)
    slope = sig * (1.0 + pre * (1.0 - sig))
    outgoing = jnp.einsum(
        "sk,kdhx->sdhx", placer, act_tiles, preferred_element_type=jnp.float32
    ).astype(jnp.bfloat16)
    outgoing, slope = lax.optimization_barrier((outgoing, slope))

    upstream = jnp.take(upstream_slots, slot_ids, axis=0, mode="clip")
    mask = occupancy.astype(jnp.float32)
    plane_mask = jnp.repeat(mask, TD)
    grad_pre = upstream.reshape(count * TD, TH, TW, C).astype(jnp.float32) * slope
    grad_pre = grad_pre * plane_mask[:, None, None, None]
    grad_pre = grad_pre.astype(jnp.bfloat16)
    back = conv_input_grad(grad_pre, kernel)
    wgrad = conv_kernel_grad(planes, grad_pre).reshape(9 * C, C)
    back = back * plane_mask[:, None, None, None]
    input_grad = back.astype(jnp.bfloat16).reshape(count, TD, TH, TW * C)

    flat_w = wgrad.reshape(n_slab, -1)
    high = lax.reduce_precision(flat_w, exponent_bits=8, mantissa_bits=7)
    low = flat_w - high
    share_width = flat_w.shape[1]
    plane = TH * TW * C
    extra = -(-2 * share_width // plane)
    pair = jnp.concatenate([high, low], axis=1).astype(jnp.bfloat16)
    pair = jnp.pad(pair, ((0, 0), (0, extra * plane - 2 * share_width)))
    pair = pair.reshape(n_slab, extra, TH, TW * C)
    act_rows = outgoing.reshape(n_slab, capacity * TD, TH, TW * C)
    payload = jnp.concatenate([act_rows, pair], axis=1)
    arrived = lax.all_to_all(payload, "slab", split_axis=0, concat_axis=0, tiled=True)
    activations = arrived[:, : capacity * TD].reshape(outgoing.shape)
    got = arrived[:, capacity * TD :].reshape(n_slab, -1)[:, : 2 * share_width].astype(jnp.float32)
    share = jnp.sum(got[:, :share_width], axis=0) + jnp.sum(got[:, share_width:], axis=0)
    share = over_copies(share, "grp")
    summed = gathered_copies(share, "slab", 0).reshape(9 * C, C)
    scale = 1.0 / math.sqrt(per_owner * n_group * n_slab * TD * TH * TW)
    return (activations, input_grad, summed * scale)


def solution(mesh):
    in_specs = (
        P(("grp", "slab"), None, None, None),
        P(),
        P(("grp", "slab"), None),
        P(("grp", "slab")),
        P(("grp", "slab"), None, None, None),
    )
    out_specs = (P(("grp", "slab"), None, None, None), P(("grp", "slab"), None, None, None), P())
    return jax.shard_map(local, mesh=mesh, in_specs=in_specs, out_specs=out_specs, check_vma=False)
```

```python
import math

import jax
import jax.numpy as jnp
from jax import lax
from jax.sharding import PartitionSpec as P

C = 64
TD = 2
TH = 8
TW = 8


def cut_along(x, dim, size):
    before, after = (x.shape[:dim], x.shape[dim + 1 :])
    return jnp.moveaxis(x.reshape(*before, size, -1, *after), dim, 0)


def sent_and_summed(x, axis, dim):
    size = lax.axis_size(axis)
    pieces = lax.all_to_all(cut_along(x, dim, size), axis, 0, 0, tiled=True)
    return jnp.sum(pieces, axis=0)


def sent_to_all(x, axis):
    size = lax.axis_size(axis)
    return lax.all_to_all(jnp.broadcast_to(x[None], (size, *x.shape)), axis, 0, 0, tiled=True)


def over_copies(x, axis):
    everything = sent_to_all(x, axis)
    return jnp.sum(everything, axis=0)


def joined_along(pieces, dim):
    pieces = jnp.moveaxis(pieces, 0, dim)
    dims = pieces.shape
    return pieces.reshape(*dims[:dim], dims[dim] * dims[dim + 1], *dims[dim + 2 :])


def gathered_copies(x, axis, dim):
    return joined_along(sent_to_all(x, axis), dim)


def conv_forward(planes, kernel):
    return lax.conv_general_dilated(
        planes,
        kernel,
        (1, 1),
        ((1, 1), (1, 1)),
        dimension_numbers=("NHWC", "HWIO", "NHWC"),
        preferred_element_type=jnp.float32,
    )


def conv_input_grad(grad_planes, kernel):
    flipped = jnp.transpose(kernel[::-1, ::-1, :, :], (0, 1, 3, 2))
    return lax.conv_general_dilated(
        grad_planes,
        flipped,
        (1, 1),
        ((1, 1), (1, 1)),
        dimension_numbers=("NHWC", "HWIO", "NHWC"),
        preferred_element_type=jnp.float32,
    )


def conv_kernel_grad(planes, grad_planes):
    return lax.conv_general_dilated(
        planes,
        grad_planes,
        (1, 1),
        ((1, 1), (1, 1)),
        dimension_numbers=("CHWN", "IHWO", "HWNC"),
        preferred_element_type=jnp.float32,
    )


def local(tiles, conv_weight, assignment, occupancy, cotangent):
    n_slab = lax.axis_size("slab")
    n_group = lax.axis_size("grp")
    per_owner = tiles.shape[0]
    capacity = max(2, -(-per_owner // n_slab))
    slot_count = n_slab * capacity
    targets = assignment[:, 0]
    same = targets[:, None] == targets[None, :]
    before = jnp.arange(per_owner)[None, :] < jnp.arange(per_owner)[:, None]
    ranks = jnp.sum((same & before).astype(jnp.int32), axis=1)
    slot_ids = targets * capacity + ranks
    placer = (
        (jnp.arange(slot_count)[:, None] == slot_ids[None, :]) & (occupancy[None, :] == 1)
    ).astype(jnp.bfloat16)
    upstream_slots = lax.all_to_all(cotangent, "slab", split_axis=0, concat_axis=0, tiled=True)

    count = per_owner
    lanes = TW * C
    kernel = conv_weight.reshape(3, 3, C, C)
    shifts = (jnp.arange(TW)[None, :, None] == jnp.arange(TW)[None, None, :] + jnp.arange(3)[:, None, None] - 1)
    band = jnp.einsum(
        "bwv,abco->awcvo", shifts.astype(jnp.bfloat16), kernel, preferred_element_type=jnp.float32
    ).astype(jnp.bfloat16).reshape(3, lanes, lanes)
    planes = tiles.reshape(count * TD, TH, lanes)
    padded = jnp.pad(planes, ((0, 0), (1, 1), (0, 0)))
    rows_at = [padded[:, a : a + TH, :].reshape(-1, lanes) for a in range(3)]
    pre = sum(
        jnp.dot(rows_at[a], band[a], preferred_element_type=jnp.float32) for a in range(3)
    )

    sig = jax.nn.sigmoid(pre)
    act_tiles = (pre * sig).astype(jnp.bfloat16).reshape(count, TD, TH, lanes)
    slope = sig * (1.0 + pre * (1.0 - sig))
    outgoing = jnp.einsum(
        "sk,kdhx->sdhx", placer, act_tiles, preferred_element_type=jnp.float32
    ).astype(jnp.bfloat16)
    outgoing, slope = lax.optimization_barrier((outgoing, slope))

    upstream = jnp.take(upstream_slots, slot_ids, axis=0, mode="clip")
    row_mask = jnp.repeat(occupancy.astype(jnp.float32), TD * TH)[:, None]
    grad_pre = (upstream.reshape(-1, lanes).astype(jnp.float32) * slope * row_mask).astype(jnp.bfloat16)

    picks = shifts.astype(jnp.float32)[:, :, None, :, None]
    pieces = []
    for a in range(3):
        block = jnp.dot(rows_at[a].T, grad_pre, preferred_element_type=jnp.float32)
        block = block.reshape(1, TW, C, TW, C)
        pieces.append(jnp.sum(block * picks, axis=(1, 3)))
    wgrad = jnp.stack(pieces).reshape(9 * C, C)

    grad_planes = jnp.pad(grad_pre.reshape(count * TD, TH, lanes), ((0, 0), (1, 1), (0, 0)))
    back = sum(
        lax.dot_general(
            grad_planes[:, 2 - a : 2 - a + TH, :].reshape(-1, lanes),
            band[a],
            (((1,), (1,)), ((), ())),
            preferred_element_type=jnp.float32,
        )
        for a in range(3)
    )
    input_grad = (back * row_mask).astype(jnp.bfloat16).reshape(count, TD, TH, lanes)

    flat_w = wgrad.reshape(n_slab, -1)
    high = lax.reduce_precision(flat_w, exponent_bits=8, mantissa_bits=7)
    low = flat_w - high
    share_width = flat_w.shape[1]
    plane = TH * TW * C
    extra = -(-2 * share_width // plane)
    pair = jnp.concatenate([high, low], axis=1).astype(jnp.bfloat16)
    pair = jnp.pad(pair, ((0, 0), (0, extra * plane - 2 * share_width)))
    pair = pair.reshape(n_slab, extra, TH, TW * C)
    act_rows = outgoing.reshape(n_slab, capacity * TD, TH, TW * C)
    payload = jnp.concatenate([act_rows, pair], axis=1)
    arrived = lax.all_to_all(payload, "slab", split_axis=0, concat_axis=0, tiled=True)
    activations = arrived[:, : capacity * TD].reshape(outgoing.shape)
    got = arrived[:, capacity * TD :].reshape(n_slab, -1)[:, : 2 * share_width].astype(jnp.float32)
    share = jnp.sum(got[:, :share_width], axis=0) + jnp.sum(got[:, share_width:], axis=0)
    share = over_copies(share, "grp")
    summed = gathered_copies(share, "slab", 0).reshape(9 * C, C)
    scale = 1.0 / math.sqrt(per_owner * n_group * n_slab * TD * TH * TW)
    return (activations, input_grad, summed * scale)


def solution(mesh):
    in_specs = (
        P(("grp", "slab"), None, None, None),
        P(),
        P(("grp", "slab"), None),
        P(("grp", "slab")),
        P(("grp", "slab"), None, None, None),
    )
    out_specs = (P(("grp", "slab"), None, None, None), P(("grp", "slab"), None, None, None), P())
    return jax.shard_map(local, mesh=mesh, in_specs=in_specs, out_specs=out_specs, check_vma=False)
```

```python
import math

import jax
import jax.numpy as jnp
from jax import lax
from jax.sharding import PartitionSpec as P

C = 64
TD = 2
TH = 8
TW = 8


def cut_along(x, dim, size):
    before, after = (x.shape[:dim], x.shape[dim + 1 :])
    return jnp.moveaxis(x.reshape(*before, size, -1, *after), dim, 0)


def sent_and_summed(x, axis, dim):
    size = lax.axis_size(axis)
    pieces = lax.all_to_all(cut_along(x, dim, size), axis, 0, 0, tiled=True)
    return jnp.sum(pieces, axis=0)


def sent_to_all(x, axis):
    size = lax.axis_size(axis)
    return lax.all_to_all(jnp.broadcast_to(x[None], (size, *x.shape)), axis, 0, 0, tiled=True)


def over_copies(x, axis):
    everything = sent_to_all(x, axis)
    return jnp.sum(everything, axis=0)


def joined_along(pieces, dim):
    pieces = jnp.moveaxis(pieces, 0, dim)
    dims = pieces.shape
    return pieces.reshape(*dims[:dim], dims[dim] * dims[dim + 1], *dims[dim + 2 :])


def gathered_copies(x, axis, dim):
    return joined_along(sent_to_all(x, axis), dim)


def conv_forward(planes, kernel):
    return lax.conv_general_dilated(
        planes,
        kernel,
        (1, 1),
        ((1, 1), (1, 1)),
        dimension_numbers=("NHWC", "HWIO", "NHWC"),
        preferred_element_type=jnp.float32,
    )


def conv_input_grad(grad_planes, kernel):
    flipped = jnp.transpose(kernel[::-1, ::-1, :, :], (0, 1, 3, 2))
    return lax.conv_general_dilated(
        grad_planes,
        flipped,
        (1, 1),
        ((1, 1), (1, 1)),
        dimension_numbers=("NHWC", "HWIO", "NHWC"),
        preferred_element_type=jnp.float32,
    )


def conv_kernel_grad(planes, grad_planes):
    return lax.conv_general_dilated(
        planes,
        grad_planes,
        (1, 1),
        ((1, 1), (1, 1)),
        dimension_numbers=("CHWN", "IHWO", "HWNC"),
        preferred_element_type=jnp.float32,
    )


def local(tiles, conv_weight, assignment, occupancy, cotangent):
    n_slab = lax.axis_size("slab")
    n_group = lax.axis_size("grp")
    per_owner = tiles.shape[0]
    capacity = max(2, -(-per_owner // n_slab))
    slot_count = n_slab * capacity
    targets = assignment[:, 0]
    same = targets[:, None] == targets[None, :]
    before = jnp.arange(per_owner)[None, :] < jnp.arange(per_owner)[:, None]
    ranks = jnp.sum((same & before).astype(jnp.int32), axis=1)
    slot_ids = targets * capacity + ranks
    placer = (
        (jnp.arange(slot_count)[:, None] == slot_ids[None, :]) & (occupancy[None, :] == 1)
    ).astype(jnp.bfloat16)
    kernel = conv_weight.reshape(3, 3, C, C)
    upstream_slots = lax.all_to_all(cotangent, "slab", split_axis=0, concat_axis=0, tiled=True)

    count = per_owner
    planes = tiles.reshape(count * TD, TH, TW, C)
    pre = conv_forward(planes, kernel)
    sig = jax.nn.sigmoid(pre)
    act_tiles = (pre * sig).astype(jnp.bfloat16).reshape(count, TD, TH, TW * C)
    slope = sig * (1.0 + pre * (1.0 - sig))
    outgoing = jnp.einsum(
        "sk,kdhx->sdhx", placer, act_tiles, preferred_element_type=jnp.float32
    ).astype(jnp.bfloat16)
    slope = slope.reshape(count, TD, TH, TW * C)
    outgoing, slope = lax.optimization_barrier((outgoing, slope))

    upstream = jnp.take(upstream_slots, slot_ids, axis=0, mode="clip")
    mask = occupancy.astype(jnp.float32)
    plane_mask = jnp.repeat(mask, TD)
    grad_pre = upstream.astype(jnp.float32) * slope
    grad_pre = grad_pre * mask[:, None, None, None]
    grad_pre = grad_pre.astype(jnp.bfloat16).reshape(count * TD, TH, TW, C)
    back = conv_input_grad(grad_pre, kernel)
    wgrad = conv_kernel_grad(planes, grad_pre).reshape(9 * C, C)
    back = back * plane_mask[:, None, None, None]
    input_grad = back.astype(jnp.bfloat16).reshape(count, TD, TH, TW * C)

    flat_w = wgrad.reshape(n_slab, -1)
    high = lax.reduce_precision(flat_w, exponent_bits=8, mantissa_bits=7)
    low = flat_w - high
    share_width = flat_w.shape[1]
    plane = TH * TW * C
    extra = -(-2 * share_width // plane)
    pair = jnp.concatenate([high, low], axis=1).astype(jnp.bfloat16)
    pair = jnp.pad(pair, ((0, 0), (0, extra * plane - 2 * share_width)))
    pair = pair.reshape(n_slab, extra, TH, TW * C)
    act_rows = outgoing.reshape(n_slab, capacity * TD, TH, TW * C)
    payload = jnp.concatenate([act_rows, pair], axis=1)
    arrived = lax.all_to_all(payload, "slab", split_axis=0, concat_axis=0, tiled=True)
    activations = arrived[:, : capacity * TD].reshape(outgoing.shape)
    got = arrived[:, capacity * TD :].reshape(n_slab, -1)[:, : 2 * share_width].astype(jnp.float32)
    share = jnp.sum(got[:, :share_width], axis=0) + jnp.sum(got[:, share_width:], axis=0)
    share = over_copies(share, "grp")
    summed = gathered_copies(share, "slab", 0).reshape(9 * C, C)
    scale = 1.0 / math.sqrt(per_owner * n_group * n_slab * TD * TH * TW)
    return (activations, input_grad, summed * scale)


def solution(mesh):
    in_specs = (
        P(("grp", "slab"), None, None, None),
        P(),
        P(("grp", "slab"), None),
        P(("grp", "slab")),
        P(("grp", "slab"), None, None, None),
    )
    out_specs = (P(("grp", "slab"), None, None, None), P(("grp", "slab"), None, None, None), P())
    return jax.shard_map(local, mesh=mesh, in_specs=in_specs, out_specs=out_specs, check_vma=False)
```

```python
import math

import jax
import jax.numpy as jnp
from jax import lax
from jax.sharding import PartitionSpec as P

C = 64
TD = 2
TH = 8
TW = 8


def cut_along(x, dim, size):
    before, after = (x.shape[:dim], x.shape[dim + 1 :])
    return jnp.moveaxis(x.reshape(*before, size, -1, *after), dim, 0)


def sent_and_summed(x, axis, dim):
    size = lax.axis_size(axis)
    pieces = lax.all_to_all(cut_along(x, dim, size), axis, 0, 0, tiled=True)
    return jnp.sum(pieces, axis=0)


def sent_to_all(x, axis):
    size = lax.axis_size(axis)
    return lax.all_to_all(jnp.broadcast_to(x[None], (size, *x.shape)), axis, 0, 0, tiled=True)


def over_copies(x, axis):
    everything = sent_to_all(x, axis)
    return jnp.sum(everything, axis=0)


def joined_along(pieces, dim):
    pieces = jnp.moveaxis(pieces, 0, dim)
    dims = pieces.shape
    return pieces.reshape(*dims[:dim], dims[dim] * dims[dim + 1], *dims[dim + 2 :])


def gathered_copies(x, axis, dim):
    return joined_along(sent_to_all(x, axis), dim)


def conv_forward(planes, kernel):
    return lax.conv_general_dilated(
        planes,
        kernel,
        (1, 1),
        ((1, 1), (1, 1)),
        dimension_numbers=("NHWC", "HWIO", "NHWC"),
        preferred_element_type=jnp.float32,
    )


def conv_input_grad(grad_planes, kernel):
    flipped = jnp.transpose(kernel[::-1, ::-1, :, :], (0, 1, 3, 2))
    return lax.conv_general_dilated(
        grad_planes,
        flipped,
        (1, 1),
        ((1, 1), (1, 1)),
        dimension_numbers=("NHWC", "HWIO", "NHWC"),
        preferred_element_type=jnp.float32,
    )


def conv_kernel_grad(planes, grad_planes):
    return lax.conv_general_dilated(
        planes,
        grad_planes,
        (1, 1),
        ((1, 1), (1, 1)),
        dimension_numbers=("CHWN", "IHWO", "HWNC"),
        preferred_element_type=jnp.float32,
    )


def local(tiles, conv_weight, assignment, occupancy, cotangent):
    n_slab = lax.axis_size("slab")
    n_group = lax.axis_size("grp")
    per_owner = tiles.shape[0]
    capacity = max(2, -(-per_owner // n_slab))
    slot_count = n_slab * capacity
    targets = assignment[:, 0]
    same = targets[:, None] == targets[None, :]
    before = jnp.arange(per_owner)[None, :] < jnp.arange(per_owner)[:, None]
    ranks = jnp.sum((same & before).astype(jnp.int32), axis=1)
    slot_ids = targets * capacity + ranks
    placer = (
        (jnp.arange(slot_count)[:, None] == slot_ids[None, :]) & (occupancy[None, :] == 1)
    ).astype(jnp.bfloat16)
    kernel = conv_weight.reshape(3, 3, C, C)
    upstream_slots = lax.all_to_all(cotangent, "slab", split_axis=0, concat_axis=0, tiled=True)

    count = per_owner
    planes = tiles.reshape(count * TD, TH, TW, C)
    pre = conv_forward(planes, kernel)
    sig = jax.nn.sigmoid(pre)
    act_tiles = (pre * sig).astype(jnp.bfloat16).reshape(count, TD, TH, TW * C)
    slope = sig * (1.0 + pre * (1.0 - sig))
    outgoing = jnp.einsum(
        "sk,kdhx->sdhx", placer, act_tiles, preferred_element_type=jnp.float32
    ).astype(jnp.bfloat16)
    slope = slope.reshape(count, TD, TH, TW * C)
    outgoing, slope = lax.optimization_barrier((outgoing, slope))

    upstream = jnp.einsum(
        "sk,sdhx->kdhx", placer, upstream_slots, preferred_element_type=jnp.float32
    )
    mask = occupancy.astype(jnp.float32)
    plane_mask = jnp.repeat(mask, TD)
    grad_pre = upstream.astype(jnp.float32) * slope
    grad_pre = grad_pre * mask[:, None, None, None]
    grad_pre = grad_pre.astype(jnp.bfloat16).reshape(count * TD, TH, TW, C)
    back = conv_input_grad(grad_pre, kernel)
    wgrad = conv_kernel_grad(planes, grad_pre).reshape(9 * C, C)
    back = back * plane_mask[:, None, None, None]
    input_grad = back.astype(jnp.bfloat16).reshape(count, TD, TH, TW * C)

    flat_w = wgrad.reshape(n_slab, -1)
    high = lax.reduce_precision(flat_w, exponent_bits=8, mantissa_bits=7)
    low = flat_w - high
    share_width = flat_w.shape[1]
    plane = TH * TW * C
    extra = -(-2 * share_width // plane)
    pair = jnp.concatenate([high, low], axis=1).astype(jnp.bfloat16)
    pair = jnp.pad(pair, ((0, 0), (0, extra * plane - 2 * share_width)))
    pair = pair.reshape(n_slab, extra, TH, TW * C)
    act_rows = outgoing.reshape(n_slab, capacity * TD, TH, TW * C)
    payload = jnp.concatenate([act_rows, pair], axis=1)
    arrived = lax.all_to_all(payload, "slab", split_axis=0, concat_axis=0, tiled=True)
    activations = arrived[:, : capacity * TD].reshape(outgoing.shape)
    got = arrived[:, capacity * TD :].reshape(n_slab, -1)[:, : 2 * share_width].astype(jnp.float32)
    share = jnp.sum(got[:, :share_width], axis=0) + jnp.sum(got[:, share_width:], axis=0)
    scale = 1.0 / math.sqrt(per_owner * n_group * n_slab * TD * TH * TW)
    share = over_copies(share, "grp") * scale
    summed = gathered_copies(share, "slab", 0).reshape(9 * C, C)
    return (activations, input_grad, summed)


def solution(mesh):
    in_specs = (
        P(("grp", "slab"), None, None, None),
        P(),
        P(("grp", "slab"), None),
        P(("grp", "slab")),
        P(("grp", "slab"), None, None, None),
    )
    out_specs = (P(("grp", "slab"), None, None, None), P(("grp", "slab"), None, None, None), P())
    return jax.shard_map(local, mesh=mesh, in_specs=in_specs, out_specs=out_specs, check_vma=False)
```

```python
import math

import jax
import jax.numpy as jnp
from jax import lax
from jax.sharding import PartitionSpec as P

C = 64
TD = 2
TH = 8
TW = 8


def cut_along(x, dim, size):
    before, after = (x.shape[:dim], x.shape[dim + 1 :])
    return jnp.moveaxis(x.reshape(*before, size, -1, *after), dim, 0)


def sent_and_summed(x, axis, dim):
    size = lax.axis_size(axis)
    pieces = lax.all_to_all(cut_along(x, dim, size), axis, 0, 0, tiled=True)
    return jnp.sum(pieces, axis=0)


def sent_to_all(x, axis):
    size = lax.axis_size(axis)
    return lax.all_to_all(jnp.broadcast_to(x[None], (size, *x.shape)), axis, 0, 0, tiled=True)


def over_copies(x, axis):
    everything = sent_to_all(x, axis)
    return jnp.sum(everything, axis=0)


def joined_along(pieces, dim):
    pieces = jnp.moveaxis(pieces, 0, dim)
    dims = pieces.shape
    return pieces.reshape(*dims[:dim], dims[dim] * dims[dim + 1], *dims[dim + 2 :])


def gathered_copies(x, axis, dim):
    return joined_along(sent_to_all(x, axis), dim)


def conv_forward(planes, kernel):
    return lax.conv_general_dilated(
        planes,
        kernel,
        (1, 1),
        ((1, 1), (1, 1)),
        dimension_numbers=("NHWC", "HWIO", "NHWC"),
        preferred_element_type=jnp.float32,
    )


def conv_input_grad(grad_planes, kernel):
    flipped = jnp.transpose(kernel[::-1, ::-1, :, :], (0, 1, 3, 2))
    return lax.conv_general_dilated(
        grad_planes,
        flipped,
        (1, 1),
        ((1, 1), (1, 1)),
        dimension_numbers=("NHWC", "HWIO", "NHWC"),
        preferred_element_type=jnp.float32,
    )


def conv_kernel_grad(planes, grad_planes):
    return lax.conv_general_dilated(
        planes,
        grad_planes,
        (1, 1),
        ((1, 1), (1, 1)),
        dimension_numbers=("CHWN", "IHWO", "HWNC"),
        preferred_element_type=jnp.float32,
    )


def local(tiles, conv_weight, assignment, occupancy, cotangent):
    n_slab = lax.axis_size("slab")
    n_group = lax.axis_size("grp")
    per_owner = tiles.shape[0]
    capacity = max(2, -(-per_owner // n_slab))
    slot_count = n_slab * capacity
    targets = assignment[:, 0]
    same = targets[:, None] == targets[None, :]
    before = jnp.arange(per_owner)[None, :] < jnp.arange(per_owner)[:, None]
    ranks = jnp.sum((same & before).astype(jnp.int32), axis=1)
    slot_ids = targets * capacity + ranks
    placer = (
        (jnp.arange(slot_count)[:, None] == slot_ids[None, :]) & (occupancy[None, :] == 1)
    ).astype(jnp.bfloat16)
    kernel = conv_weight.reshape(3, 3, C, C)
    upstream_slots = lax.all_to_all(cotangent, "slab", split_axis=0, concat_axis=0, tiled=True)

    count = per_owner
    planes = tiles.reshape(count * TD, TH, TW, C)
    pre = conv_forward(planes, kernel)
    sig = jax.nn.sigmoid(pre)
    act_tiles = (pre * sig).astype(jnp.bfloat16).reshape(count, TD, TH, TW * C)
    slope = sig * (1.0 + pre * (1.0 - sig))
    outgoing = jnp.einsum(
        "sk,kdhx->sdhx", placer, act_tiles, preferred_element_type=jnp.float32
    ).astype(jnp.bfloat16)
    slope = slope.reshape(count, TD, TH, TW * C)
    framed = jnp.pad(planes, ((0, 0), (1, 1), (1, 1), (0, 0)))
    windows = [framed[:, a : a + TH, b : b + TW, :].reshape(-1, C) for a in range(3) for b in range(3)]
    taps = jnp.concatenate(windows, axis=1).T
    outgoing, slope, taps = lax.optimization_barrier((outgoing, slope, taps))

    upstream = jnp.take(upstream_slots, slot_ids, axis=0, mode="clip")
    mask = occupancy.astype(jnp.float32)
    plane_mask = jnp.repeat(mask, TD)
    grad_pre = upstream.astype(jnp.float32) * slope
    grad_pre = grad_pre * mask[:, None, None, None]
    grad_pre = grad_pre.astype(jnp.bfloat16).reshape(count * TD, TH, TW, C)
    back = conv_input_grad(grad_pre, kernel)
    wgrad = jnp.dot(taps, grad_pre.reshape(-1, C), preferred_element_type=jnp.float32)
    back = back * plane_mask[:, None, None, None]
    input_grad = back.astype(jnp.bfloat16).reshape(count, TD, TH, TW * C)

    flat_w = wgrad.reshape(n_slab, -1)
    high = lax.reduce_precision(flat_w, exponent_bits=8, mantissa_bits=7)
    low = flat_w - high
    share_width = flat_w.shape[1]
    plane = TH * TW * C
    extra = -(-2 * share_width // plane)
    pair = jnp.concatenate([high, low], axis=1).astype(jnp.bfloat16)
    pair = jnp.pad(pair, ((0, 0), (0, extra * plane - 2 * share_width)))
    pair = pair.reshape(n_slab, extra, TH, TW * C)
    act_rows = outgoing.reshape(n_slab, capacity * TD, TH, TW * C)
    payload = jnp.concatenate([act_rows, pair], axis=1)
    arrived = lax.all_to_all(payload, "slab", split_axis=0, concat_axis=0, tiled=True)
    activations = arrived[:, : capacity * TD].reshape(outgoing.shape)
    got = arrived[:, capacity * TD :].reshape(n_slab, -1)[:, : 2 * share_width].astype(jnp.float32)
    share = jnp.sum(got[:, :share_width], axis=0) + jnp.sum(got[:, share_width:], axis=0)
    share = over_copies(share, "grp")
    summed = gathered_copies(share, "slab", 0).reshape(9 * C, C)
    scale = 1.0 / math.sqrt(per_owner * n_group * n_slab * TD * TH * TW)
    return (activations, input_grad, summed * scale)


def solution(mesh):
    in_specs = (
        P(("grp", "slab"), None, None, None),
        P(),
        P(("grp", "slab"), None),
        P(("grp", "slab")),
        P(("grp", "slab"), None, None, None),
    )
    out_specs = (P(("grp", "slab"), None, None, None), P(("grp", "slab"), None, None, None), P())
    return jax.shard_map(local, mesh=mesh, in_specs=in_specs, out_specs=out_specs, check_vma=False)
```

```python
import math

import jax
import jax.numpy as jnp
from jax import lax
from jax.sharding import PartitionSpec as P

C = 64
TD = 2
TH = 8
TW = 8


def cut_along(x, dim, size):
    before, after = (x.shape[:dim], x.shape[dim + 1 :])
    return jnp.moveaxis(x.reshape(*before, size, -1, *after), dim, 0)


def sent_and_summed(x, axis, dim):
    size = lax.axis_size(axis)
    pieces = lax.all_to_all(cut_along(x, dim, size), axis, 0, 0, tiled=True)
    return jnp.sum(pieces, axis=0)


def sent_to_all(x, axis):
    size = lax.axis_size(axis)
    return lax.all_to_all(jnp.broadcast_to(x[None], (size, *x.shape)), axis, 0, 0, tiled=True)


def over_copies(x, axis):
    everything = sent_to_all(x, axis)
    return jnp.sum(everything, axis=0)


def joined_along(pieces, dim):
    pieces = jnp.moveaxis(pieces, 0, dim)
    dims = pieces.shape
    return pieces.reshape(*dims[:dim], dims[dim] * dims[dim + 1], *dims[dim + 2 :])


def gathered_copies(x, axis, dim):
    return joined_along(sent_to_all(x, axis), dim)


def conv_forward(planes, kernel):
    return lax.conv_general_dilated(
        planes,
        kernel,
        (1, 1),
        ((1, 1), (1, 1)),
        dimension_numbers=("NHWC", "HWIO", "NHWC"),
        preferred_element_type=jnp.float32,
    )


def conv_input_grad(grad_planes, kernel):
    flipped = jnp.transpose(kernel[::-1, ::-1, :, :], (0, 1, 3, 2))
    return lax.conv_general_dilated(
        grad_planes,
        flipped,
        (1, 1),
        ((1, 1), (1, 1)),
        dimension_numbers=("NHWC", "HWIO", "NHWC"),
        preferred_element_type=jnp.float32,
    )


def conv_kernel_grad(planes, grad_planes):
    return lax.conv_general_dilated(
        planes,
        grad_planes,
        (1, 1),
        ((1, 1), (1, 1)),
        dimension_numbers=("CHWN", "IHWO", "HWNC"),
        preferred_element_type=jnp.float32,
    )


def local(tiles, conv_weight, assignment, occupancy, cotangent):
    n_slab = lax.axis_size("slab")
    n_group = lax.axis_size("grp")
    per_owner = tiles.shape[0]
    capacity = max(2, -(-per_owner // n_slab))
    slot_count = n_slab * capacity
    targets = assignment[:, 0]
    same = targets[:, None] == targets[None, :]
    before = jnp.arange(per_owner)[None, :] < jnp.arange(per_owner)[:, None]
    ranks = jnp.sum((same & before).astype(jnp.int32), axis=1)
    slot_ids = targets * capacity + ranks
    placer = (
        (jnp.arange(slot_count)[:, None] == slot_ids[None, :]) & (occupancy[None, :] == 1)
    ).astype(jnp.bfloat16)
    kernel = conv_weight.reshape(3, 3, C, C)
    upstream_slots = lax.all_to_all(cotangent, "slab", split_axis=0, concat_axis=0, tiled=True)

    count = per_owner
    planes = tiles.reshape(count * TD, TH, TW, C)
    pre = conv_forward(planes, kernel)
    sig = jax.nn.sigmoid(pre)
    act_tiles = (pre * sig).astype(jnp.bfloat16).reshape(count, TD, TH, TW * C)
    slope = sig * (1.0 + pre * (1.0 - sig))
    outgoing = jnp.einsum(
        "sk,kdhx->sdhx", placer, act_tiles, preferred_element_type=jnp.float32
    ).astype(jnp.bfloat16)
    slope = slope.reshape(count, TD, TH, TW * C)
    outgoing, slope = lax.optimization_barrier((outgoing, slope))

    upstream = jnp.take(upstream_slots, slot_ids, axis=0, mode="clip")
    mask = occupancy.astype(jnp.float32)
    plane_mask = jnp.repeat(mask, TD)
    grad_pre = upstream.astype(jnp.float32) * slope
    grad_pre = grad_pre * mask[:, None, None, None]
    grad_pre = grad_pre.astype(jnp.bfloat16).reshape(count * TD, TH, TW, C)
    back = conv_input_grad(grad_pre, kernel)
    wgrad = conv_kernel_grad(planes, grad_pre).reshape(9 * C, C)
    back = back * plane_mask[:, None, None, None]
    input_grad = back.astype(jnp.bfloat16).reshape(count, TD, TH, TW * C)

    flat_w = wgrad.T.reshape(n_slab, -1)
    high = lax.reduce_precision(flat_w, exponent_bits=8, mantissa_bits=7)
    low = flat_w - high
    share_width = flat_w.shape[1]
    plane = TH * TW * C
    extra = -(-2 * share_width // plane)
    pair = jnp.concatenate([high, low], axis=1).astype(jnp.bfloat16)
    pair = jnp.pad(pair, ((0, 0), (0, extra * plane - 2 * share_width)))
    pair = pair.reshape(n_slab, extra, TH, TW * C)
    act_rows = outgoing.reshape(n_slab, capacity * TD, TH, TW * C)
    payload = jnp.concatenate([act_rows, pair], axis=1)
    arrived = lax.all_to_all(payload, "slab", split_axis=0, concat_axis=0, tiled=True)
    activations = arrived[:, : capacity * TD].reshape(outgoing.shape)
    got = arrived[:, capacity * TD :].reshape(n_slab, -1)[:, : 2 * share_width].astype(jnp.float32)
    share = jnp.sum(got[:, :share_width], axis=0) + jnp.sum(got[:, share_width:], axis=0)
    scale = 1.0 / math.sqrt(per_owner * n_group * n_slab * TD * TH * TW)
    share = over_copies(share, "grp") * scale
    summed = gathered_copies(share, "slab", 0).reshape(C, 9 * C).T
    return (activations, input_grad, summed)


def solution(mesh):
    in_specs = (
        P(("grp", "slab"), None, None, None),
        P(),
        P(("grp", "slab"), None),
        P(("grp", "slab")),
        P(("grp", "slab"), None, None, None),
    )
    out_specs = (P(("grp", "slab"), None, None, None), P(("grp", "slab"), None, None, None), P())
    return jax.shard_map(local, mesh=mesh, in_specs=in_specs, out_specs=out_specs, check_vma=False)
```

```python
import math

import jax
import jax.numpy as jnp
from jax import lax
from jax.sharding import PartitionSpec as P

C = 64
TD = 2
TH = 8
TW = 8


def cut_along(x, dim, size):
    before, after = (x.shape[:dim], x.shape[dim + 1 :])
    return jnp.moveaxis(x.reshape(*before, size, -1, *after), dim, 0)


def sent_and_summed(x, axis, dim):
    size = lax.axis_size(axis)
    pieces = lax.all_to_all(cut_along(x, dim, size), axis, 0, 0, tiled=True)
    return jnp.sum(pieces, axis=0)


def sent_to_all(x, axis):
    size = lax.axis_size(axis)
    return lax.all_to_all(jnp.broadcast_to(x[None], (size, *x.shape)), axis, 0, 0, tiled=True)


def over_copies(x, axis):
    everything = sent_to_all(x, axis)
    return jnp.sum(everything, axis=0)


def joined_along(pieces, dim):
    pieces = jnp.moveaxis(pieces, 0, dim)
    dims = pieces.shape
    return pieces.reshape(*dims[:dim], dims[dim] * dims[dim + 1], *dims[dim + 2 :])


def gathered_copies(x, axis, dim):
    return joined_along(sent_to_all(x, axis), dim)


def conv_forward(planes, kernel):
    return lax.conv_general_dilated(
        planes,
        kernel,
        (1, 1),
        ((1, 1), (1, 1)),
        dimension_numbers=("NHWC", "HWIO", "NHWC"),
        preferred_element_type=jnp.float32,
    )


def conv_input_grad(grad_planes, kernel):
    flipped = jnp.transpose(kernel[::-1, ::-1, :, :], (0, 1, 3, 2))
    return lax.conv_general_dilated(
        grad_planes,
        flipped,
        (1, 1),
        ((1, 1), (1, 1)),
        dimension_numbers=("NHWC", "HWIO", "NHWC"),
        preferred_element_type=jnp.float32,
    )


def conv_kernel_grad(planes, grad_planes):
    return lax.conv_general_dilated(
        planes,
        grad_planes,
        (1, 1),
        ((1, 1), (1, 1)),
        dimension_numbers=("CHWN", "IHWO", "HWNC"),
        preferred_element_type=jnp.float32,
    )


def local(tiles, conv_weight, assignment, occupancy, cotangent):
    n_slab = lax.axis_size("slab")
    n_group = lax.axis_size("grp")
    per_owner = tiles.shape[0]
    capacity = max(2, -(-per_owner // n_slab))
    slot_count = n_slab * capacity
    targets = assignment[:, 0]
    same = targets[:, None] == targets[None, :]
    before = jnp.arange(per_owner)[None, :] < jnp.arange(per_owner)[:, None]
    ranks = jnp.sum((same & before).astype(jnp.int32), axis=1)
    slot_ids = targets * capacity + ranks
    placer = (
        (jnp.arange(slot_count)[:, None] == slot_ids[None, :]) & (occupancy[None, :] == 1)
    ).astype(jnp.bfloat16)
    kernel = conv_weight.reshape(3, 3, C, C)
    upstream_slots = lax.all_to_all(cotangent, "slab", split_axis=0, concat_axis=0, tiled=True)

    count = per_owner
    planes = tiles.reshape(count * TD, TH, TW, C)
    pre = conv_forward(planes, kernel)
    sig = jax.nn.sigmoid(pre)
    act_tiles = (pre * sig).astype(jnp.bfloat16).reshape(count, TD, TH, TW * C)
    slope = sig * (1.0 + pre * (1.0 - sig))
    outgoing = jnp.einsum(
        "sk,kdhx->sdhx", placer, act_tiles, preferred_element_type=jnp.float32
    ).astype(jnp.bfloat16)
    slope = slope.reshape(count, TD, TH, TW * C)
    outgoing, slope = lax.optimization_barrier((outgoing, slope))

    upstream = jnp.take(upstream_slots, slot_ids, axis=0, mode="clip")
    mask = occupancy.astype(jnp.float32)
    plane_mask = jnp.repeat(mask, TD)
    grad_pre = upstream.astype(jnp.float32) * slope
    grad_pre = grad_pre * mask[:, None, None, None]
    grad_pre = grad_pre.astype(jnp.bfloat16).reshape(count * TD, TH, TW, C)
    back = conv_input_grad(grad_pre, kernel)
    wgrad = conv_kernel_grad(planes, grad_pre).reshape(9 * C, C)
    back = back * plane_mask[:, None, None, None]
    input_grad = back.astype(jnp.bfloat16).reshape(count, TD, TH, TW * C)

    scale = 1.0 / math.sqrt(per_owner * n_group * n_slab * TD * TH * TW)
    flat_w = (wgrad * scale).T.reshape(n_slab, -1)
    high = lax.reduce_precision(flat_w, exponent_bits=8, mantissa_bits=7)
    low = flat_w - high
    share_width = flat_w.shape[1]
    plane = TH * TW * C
    extra = -(-2 * share_width // plane)
    pair = jnp.concatenate([high, low], axis=1).astype(jnp.bfloat16)
    pair = jnp.pad(pair, ((0, 0), (0, extra * plane - 2 * share_width)))
    pair = pair.reshape(n_slab, extra, TH, TW * C)
    act_rows = outgoing.reshape(n_slab, capacity * TD, TH, TW * C)
    payload = jnp.concatenate([act_rows, pair], axis=1)
    arrived = lax.all_to_all(payload, "slab", split_axis=0, concat_axis=0, tiled=True)
    activations = arrived[:, : capacity * TD].reshape(outgoing.shape)
    got = arrived[:, capacity * TD :].reshape(n_slab, -1)[:, : 2 * share_width].astype(jnp.float32)
    share = jnp.sum(got[:, :share_width], axis=0) + jnp.sum(got[:, share_width:], axis=0)
    share = over_copies(share, "grp")
    summed = gathered_copies(share, "slab", 0).reshape(C, 9 * C).T
    return (activations, input_grad, summed)


def solution(mesh):
    in_specs = (
        P(("grp", "slab"), None, None, None),
        P(),
        P(("grp", "slab"), None),
        P(("grp", "slab")),
        P(("grp", "slab"), None, None, None),
    )
    out_specs = (P(("grp", "slab"), None, None, None), P(("grp", "slab"), None, None, None), P())
    return jax.shard_map(local, mesh=mesh, in_specs=in_specs, out_specs=out_specs, check_vma=False)
```
